512 devices in a mesh: ref: 16 (over y_hi, x, core), dom: 32 (over y_lo, z).
Axes of the slice: x: 4, y: 4 (y_hi: 2, y_lo: 2; y = y_hi * 2 + y_lo), z: 16, core: 2. Of those that a mesh axis runs over, the one named last changes fastest.
Arguments:
- particles: bfloat16 [16384, 4096], P(('ref', 'dom'))
- inv_noise: float32 [16384], P(('ref', 'dom')), may hold values from 1 to 6
- candidates: int32 [16384, 8], P(('ref', 'dom')), may hold values from 0 to 127, as said below
- offsets: int32 [9, 2], replicated, may hold values from -2 to 2, as said below
- references: bfloat16 [128, 4096], P('ref')
Outputs:
- refreshed: bfloat16 [128, 4096], P('ref', 'dom')
- log_evidence: float32 [16384], P(('ref', 'dom'))
The draws below stay inside these ranges and needn't reach their ends.
Inputs may be any that keep to these rules, and one draw needn't show every extreme that they name: `candidates`: each row names 8 different classes; class loads are uneven. `offsets`: 9 different shifts.
All inputs are finite; a program needn't handle non-finite values.
Results may differ from the reference program's by a relative error of at most 0.0038.
Values may be sent and summed in bfloat16 or wider, within the bound.
No kernel may reach another device: no remote copies, remote signals or barrier semaphores. Data moves between devices by JAX's collectives and lax.ppermute only.
A program may use at most 64 MiB of HBM per device.

```python
import math
import jax
import jax.numpy as jnp
from jax import lax

SIDE = 64
PIX = 4096
K = 128
SHIFTS = 9
CAND = 8
P_DEV = 32
PARTICLES = 16384


def class_choice(key):
    base = jax.random.randint(jax.random.fold_in(key, 3), (K,), 0, 6)
    popular = base * 8192
    noise = jax.random.randint(jax.random.fold_in(key, 4), (PARTICLES, K), 0, 65536)
    ranked = (noise + popular[None, :]) * K + jnp.arange(K, dtype=jnp.int32)[None, :]
    return lax.top_k(ranked, CAND)[1].astype(jnp.int32)


def shift_choice(key):
    order = jax.random.permutation(jax.random.fold_in(key, 5), jnp.arange(25, dtype=jnp.int32))[:SHIFTS]
    return jnp.stack([order // 5 - 2, order % 5 - 2], axis=1).astype(jnp.int32)


def ref_images(key):
    return jax.random.normal(jax.random.fold_in(key, 11), (K, PIX), jnp.float32) / SIDE


def draw_candidates(key, part):
    return class_choice(key)


def draw_offsets(key, part):
    return shift_choice(key)


def draw_references(key, part):
    return ref_images(key).astype(jnp.bfloat16)


def draw_particles(key, part):
    return jax.random.normal(jax.random.fold_in(key, 21), (PARTICLES, PIX), jnp.float32).astype(jnp.bfloat16)


def block_scale(own_key, shape, split, least, largest):
    loudness, own = 1.0, jax.random.fold_in(own_key, 6)
    for position, blocks in split:
        heights = jnp.exp(jax.random.uniform(jax.random.fold_in(own, position), (blocks,), jnp.float32, least / len(split), largest / len(split)))
        loudness = loudness * jnp.repeat(heights, shape[position] // blocks).reshape([-1 if axis == position else 1 for axis in range(len(shape))])
    return loudness


def setup_inputs(seed: int = 0) -> dict:
    keys = jax.random.split(jax.random.key(seed), 6)
    return {
        "particles": draw_particles(jax.random.fold_in(keys[5], 71), 0),
        "inv_noise": jnp.clip(jnp.exp(math.log(6.0) - 1.7917595 * jax.random.uniform(keys[1], (PARTICLES,), jnp.float32) ** block_scale(keys[1], (PARTICLES,), ((0, 512),), -0.2, 0.2)), 1.0, 6.0),
        "candidates": draw_candidates(jax.random.fold_in(keys[5], 71), 0),
        "offsets": draw_offsets(jax.random.fold_in(keys[5], 71), 0),
        "references": draw_references(jax.random.fold_in(keys[5], 71), 0),
    }


def roll_set(images, offsets, sign):
    grid = images.reshape(images.shape[0], SIDE, SIDE)

    def one_shift(offset_pair):
        return jnp.roll(grid, (sign * offset_pair[0], sign * offset_pair[1]), axis=(1, 2))
    return jax.vmap(one_shift)(offsets).reshape(offsets.shape[0], images.shape[0], PIX)

def reference(particles, inv_noise, candidates, offsets, references):
    translated_image = roll_set(references, offsets, 1).astype(jnp.float32)
    ref_float = references.astype(jnp.float32)
    norms = lax.optimization_barrier(jnp.sum(ref_float * ref_float, axis=1))
    block = 2 * P_DEV
    steps_count = PARTICLES // block
    classes = jnp.arange(K, dtype=jnp.int32)

    def one_block(running, index):
        leading_row = (index * block).astype(jnp.int32)
        part_block = lax.dynamic_slice_in_dim(particles, leading_row, block, 0)
        beta = lax.dynamic_slice_in_dim(inv_noise, leading_row, block, 0)
        cand = lax.dynamic_slice_in_dim(candidates, leading_row, block, 0)
        match_score = jnp.einsum('bq,skq->bsk', part_block.astype(jnp.float32), translated_image)
        score = beta[:, None, None] * (match_score - 0.5 * norms[None, None, :])
        permitted_mask = jnp.any(cand[:, :, None] == classes[None, None, :], axis=1)
        masked = jnp.where(permitted_mask[:, None, :], score, -1e+30)
        peak_val = lax.optimization_barrier(jnp.max(masked, axis=(1, 2)))
        denom_sum = lax.optimization_barrier(jnp.sum(jnp.exp(masked - peak_val[:, None, None]), axis=(1, 2)))
        evidence = peak_val + jnp.log(denom_sum)
        weight = jnp.where(permitted_mask[:, None, :], jnp.exp(masked - evidence[:, None, None]), 0.0).astype(jnp.bfloat16)
        stacked = roll_set(part_block, offsets, -1).astype(jnp.float32)
        running = running + jnp.einsum('bsk,sbq->kq', weight.astype(jnp.float32), stacked)
        return (running, evidence)
    class_total, evidence = lax.scan(one_block, jnp.zeros((K, PIX), jnp.float32), jnp.arange(steps_count, dtype=jnp.int32))
    row_power = lax.optimization_barrier(jnp.sum(class_total * class_total, axis=1))
    refreshed = (class_total / jnp.sqrt(row_power[:, None] / PIX + 1e-06)).astype(jnp.bfloat16)
    return (refreshed, evidence.reshape(PARTICLES))
```

```python
import jax
import jax.numpy as jnp
from jax import lax
from jax.sharding import Mesh
from jax.sharding import PartitionSpec as P

SIDE = 64
REF = ("yh", "x", "c")
DOM = ("yl", "z")
ALL = REF + DOM
HALVING = (
    ("c", 2, 1),
    ("yl", 2, 1),
    ("x", 4, 1),
    ("z", 16, 1),
    ("yh", 2, 1),
    ("x", 4, 2),
    ("z", 16, 2),
    ("z", 16, 4),
    ("z", 16, 8),
)
DOUBLING = (("yl", 2, 1), ("z", 16, 1), ("z", 16, 2), ("z", 16, 4), ("z", 16, 8))


def flat_roll(images, row_move, col_move):
    pixels = SIDE * SIDE
    moved = jnp.roll(images, row_move * SIDE, axis=1)
    col_mod = jnp.mod(col_move, SIDE)
    column = jnp.arange(pixels, dtype=jnp.int32) % SIDE
    inside = jnp.roll(moved, col_mod, axis=1)
    wrapped = jnp.roll(moved, col_mod - SIDE, axis=1)
    return jnp.where((column >= col_mod)[None, :], inside, wrapped)


def roll_set(images, offsets, sign):
    translated_image = []
    for shift_idx in range(offsets.shape[0]):
        translated_image.append(
            flat_roll(images, sign * offsets[shift_idx, 0], sign * offsets[shift_idx, 1])
        )
    return jnp.stack(translated_image, axis=1)


def partner(axis, size, bit):
    return [(i, i ^ bit) for i in range(size)]


def reduce_blocks(partial):
    t = partial.reshape(2, 2, 2, 2, 8, 2, 2, 2, 2, 2, 128)
    t = t.transpose(3, 5, 2, 9, 0, 1, 8, 7, 6, 4, 10)
    for axis, size, bit in HALVING:
        mine = (lax.axis_index(axis) // bit) % 2
        keep = lax.dynamic_index_in_dim(t, mine, 0, keepdims=False)
        send = lax.dynamic_index_in_dim(t, 1 - mine, 0, keepdims=False)
        t = keep + lax.ppermute(send, axis, partner(axis, size, bit))
    return t


def per_device(particles, inv_noise, candidates, offsets, references):
    tile_size = references.shape[0]
    all_classes = tile_size * 16
    stacked = roll_set(particles, offsets, -1)
    tile_rows = lax.all_gather(references, REF, axis=0, tiled=True)
    tile_float = tile_rows.astype(jnp.float32)
    norms = jnp.sum(tile_float * tile_float, axis=1)
    translated_image = roll_set(tile_rows, offsets, 1)
    match_score = jnp.einsum(
        "vi,jti->vtj", particles, translated_image, preferred_element_type=jnp.float32
    )
    update = match_score - 0.5 * norms[None, None, :]
    score = inv_noise[:, None, None] * update
    classes = jnp.arange(all_classes, dtype=jnp.int32)
    permitted_mask = jnp.any(candidates[:, :, None] == classes[None, None, :], axis=1)
    masked = jnp.where(permitted_mask[:, None, :], score, -1e30)
    peak_val = jnp.max(masked, axis=(1, 2))
    denom_sum = jnp.sum(jnp.exp(masked - peak_val[:, None, None]), axis=(1, 2))
    evidence = peak_val + jnp.log(denom_sum)
    weight = jnp.where(
        permitted_mask[:, None, :], jnp.exp(masked - evidence[:, None, None]), 0.0
    ).astype(jnp.bfloat16)
    partial = jnp.einsum("psk,psq->kq", weight, stacked, preferred_element_type=jnp.float32)
    shares = reduce_blocks(partial)
    row_power = jnp.sum(shares * shares, axis=1)
    for axis, size, bit in DOUBLING:
        row_power = row_power + lax.ppermute(row_power, axis, partner(axis, size, bit))
    refreshed = (shares / jnp.sqrt(row_power[:, None] / (SIDE * SIDE) + 1e-06)).astype(jnp.bfloat16)
    return (refreshed, evidence)


def solution(mesh):
    assert mesh.devices.shape == (16, 32)
    fine = Mesh(mesh.devices.reshape(2, 4, 2, 2, 16), ALL)
    in_specs = (
        P(ALL, None),
        P(ALL),
        P(ALL, None),
        P(),
        P(REF, None),
    )
    out_specs = (P(REF, DOM), P(ALL))
    return jax.shard_map(
        per_device, mesh=fine, in_specs=in_specs, out_specs=out_specs, check_vma=False
    )
```

```python
import jax
import jax.numpy as jnp
from jax import lax
from jax.sharding import Mesh
from jax.sharding import PartitionSpec as P

SIDE = 64
REF = ("yh", "x", "c")
DOM = ("yl", "z")
ALL = REF + DOM
HALVING = (
    ("c", 2, 1),
    ("yl", 2, 1),
    ("x", 4, 1),
    ("z", 16, 1),
    ("yh", 2, 1),
    ("x", 4, 2),
)
SUMMING = (("z", 16, 2), ("z", 16, 4), ("z", 16, 8))
DOUBLING = (("yl", 2, 1), ("z", 16, 1))
GATHER = (("x", 4, 2), ("yh", 2, 1), ("x", 4, 1), ("c", 2, 1))


def flat_roll(images, row_move, col_move):
    pixels = SIDE * SIDE
    moved = jnp.roll(images, row_move * SIDE, axis=1)
    col_mod = jnp.mod(col_move, SIDE)
    column = jnp.arange(pixels, dtype=jnp.int32) % SIDE
    inside = jnp.roll(moved, col_mod, axis=1)
    wrapped = jnp.roll(moved, col_mod - SIDE, axis=1)
    return jnp.where((column >= col_mod)[None, :], inside, wrapped)


def roll_set(images, offsets, sign):
    translated_image = []
    for shift_idx in range(offsets.shape[0]):
        translated_image.append(
            flat_roll(images, sign * offsets[shift_idx, 0], sign * offsets[shift_idx, 1])
        )
    return jnp.stack(translated_image, axis=1)


def partner(axis, size, bit):
    return [(i, i ^ bit) for i in range(size)]


def reduce_blocks(partial):
    t = partial.reshape(2, 2, 2, 2, 8, 2, 2, 2, 2, 2, 128)
    t = t.transpose(3, 5, 2, 9, 0, 1, 8, 7, 6, 4, 10)
    for axis, size, bit in HALVING:
        mine = (lax.axis_index(axis) // bit) % 2
        keep = lax.dynamic_index_in_dim(t, mine, 0, keepdims=False)
        send = lax.dynamic_index_in_dim(t, 1 - mine, 0, keepdims=False)
        t = keep + lax.ppermute(send, axis, partner(axis, size, bit))
    for axis, size, bit in SUMMING:
        t = t + lax.ppermute(t, axis, partner(axis, size, bit))
    return t


def gather_rows(rows):
    buf = rows
    for axis, size, bit in GATHER:
        mine = (lax.axis_index(axis) // bit) % 2
        recv = lax.ppermute(buf, axis, partner(axis, size, bit))
        buf = jnp.stack([jnp.where(mine == 0, buf, recv), jnp.where(mine == 0, recv, buf)])
    return buf.transpose(2, 3, 1, 0, 4, 5).reshape(-1, rows.shape[1])


def per_device(particles, inv_noise, candidates, offsets, references):
    tile_size = references.shape[0]
    all_classes = tile_size * 16
    stacked = roll_set(particles, offsets, -1)
    tile_rows = gather_rows(references)
    tile_float = tile_rows.astype(jnp.float32)
    norms = jnp.sum(tile_float * tile_float, axis=1)
    translated_image = roll_set(tile_rows, offsets, 1)
    match_score = jnp.einsum(
        "vi,jti->vtj", particles, translated_image, preferred_element_type=jnp.float32
    )
    update = match_score - 0.5 * norms[None, None, :]
    score = inv_noise[:, None, None] * update
    classes = jnp.arange(all_classes, dtype=jnp.int32)
    permitted_mask = jnp.any(candidates[:, :, None] == classes[None, None, :], axis=1)
    masked = jnp.where(permitted_mask[:, None, :], score, -1e30)
    peak_val = jnp.max(masked, axis=(1, 2))
    denom_sum = jnp.sum(jnp.exp(masked - peak_val[:, None, None]), axis=(1, 2))
    evidence = peak_val + jnp.log(denom_sum)
    weight = jnp.where(
        permitted_mask[:, None, :], jnp.exp(masked - evidence[:, None, None]), 0.0
    ).astype(jnp.bfloat16)
    partial = jnp.einsum("psk,psq->kq", weight, stacked, preferred_element_type=jnp.float32)
    spans = reduce_blocks(partial)
    row_power = jnp.sum(spans * spans, axis=(0, 1, 2, 4))
    for axis, size, bit in DOUBLING:
        row_power = row_power + lax.ppermute(row_power, axis, partner(axis, size, bit))
    z = lax.axis_index("z")
    shares = spans[(z // 2) % 2, (z // 4) % 2, (z // 8) % 2]
    refreshed = (shares / jnp.sqrt(row_power[:, None] / (SIDE * SIDE) + 1e-06)).astype(jnp.bfloat16)
    return (refreshed, evidence)


def solution(mesh):
    assert mesh.devices.shape == (16, 32)
    fine = Mesh(mesh.devices.reshape(2, 4, 2, 2, 16), ALL)
    in_specs = (
        P(ALL, None),
        P(ALL),
        P(ALL, None),
        P(),
        P(REF, None),
    )
    out_specs = (P(REF, DOM), P(ALL))
    return jax.shard_map(
        per_device, mesh=fine, in_specs=in_specs, out_specs=out_specs, check_vma=False
    )
```

```python
import jax
import jax.numpy as jnp
from jax import lax
from jax.sharding import Mesh
from jax.sharding import PartitionSpec as P

SIDE = 64
REF = ("yh", "x", "c")
DOM = ("yl", "z")
ALL = REF + DOM
HALVING = (
    ("c", 2, 1),
    ("yl", 2, 1),
    ("x", 4, 1),
    ("yh", 2, 1),
    ("x", 4, 2),
)


def flat_roll(images, row_move, col_move):
    pixels = SIDE * SIDE
    moved = jnp.roll(images, row_move * SIDE, axis=1)
    col_mod = jnp.mod(col_move, SIDE)
    column = jnp.arange(pixels, dtype=jnp.int32) % SIDE
    inside = jnp.roll(moved, col_mod, axis=1)
    wrapped = jnp.roll(moved, col_mod - SIDE, axis=1)
    return jnp.where((column >= col_mod)[None, :], inside, wrapped)


def roll_set(images, offsets, sign):
    translated_image = []
    for shift_idx in range(offsets.shape[0]):
        translated_image.append(
            flat_roll(images, sign * offsets[shift_idx, 0], sign * offsets[shift_idx, 1])
        )
    return jnp.stack(translated_image, axis=1)


def partner(axis, size, bit):
    return [(i, i ^ bit) for i in range(size)]


def reduce_blocks(partial):
    t = partial.reshape(2, 2, 2, 2, 8, 2, 2, 2, 2, 2, 128)
    t = t.transpose(3, 5, 2, 0, 1, 6, 7, 8, 9, 4, 10)
    for axis, size, bit in HALVING:
        mine = (lax.axis_index(axis) // bit) % 2
        keep = lax.dynamic_index_in_dim(t, mine, 0, keepdims=False)
        send = lax.dynamic_index_in_dim(t, 1 - mine, 0, keepdims=False)
        t = keep + lax.ppermute(send, axis, partner(axis, size, bit))
    t = t.reshape(-1, *t.shape[-2:])
    return jnp.sum(lax.all_to_all(t, "z", 0, 0, tiled=True), axis=0)


def gather_rows(rows):
    copies = jnp.broadcast_to(rows[None], (16, *rows.shape))
    return lax.all_to_all(copies, REF, 0, 0, tiled=True).reshape(-1, rows.shape[1])


def per_device(particles, inv_noise, candidates, offsets, references):
    tile_size = references.shape[0]
    all_classes = tile_size * 16
    stacked = roll_set(particles, offsets, -1)
    tile_rows = gather_rows(references)
    tile_float = tile_rows.astype(jnp.float32)
    norms = jnp.sum(tile_float * tile_float, axis=1)
    translated_image = roll_set(tile_rows, offsets, 1)
    match_score = jnp.einsum(
        "vi,jti->vtj", particles, translated_image, preferred_element_type=jnp.float32
    )
    update = match_score - 0.5 * norms[None, None, :]
    score = inv_noise[:, None, None] * update
    classes = jnp.arange(all_classes, dtype=jnp.int32)
    permitted_mask = jnp.any(candidates[:, :, None] == classes[None, None, :], axis=1)
    masked = jnp.where(permitted_mask[:, None, :], score, -1e30)
    peak_val = jnp.max(masked, axis=(1, 2))
    denom_sum = jnp.sum(jnp.exp(masked - peak_val[:, None, None]), axis=(1, 2))
    evidence = peak_val + jnp.log(denom_sum)
    weight = jnp.where(
        permitted_mask[:, None, :], jnp.exp(masked - evidence[:, None, None]), 0.0
    ).astype(jnp.bfloat16)
    partial = jnp.einsum("psk,psq->kq", weight, stacked, preferred_element_type=jnp.float32)
    shares = reduce_blocks(partial)
    row_power = jnp.sum(shares * shares, axis=1)
    row_power = row_power + lax.ppermute(row_power, "yl", partner("yl", 2, 1))
    row_power = jnp.broadcast_to(row_power[None], (16, row_power.shape[0]))
    row_power = jnp.sum(lax.all_to_all(row_power, "z", 0, 0, tiled=True), axis=0)
    refreshed = (shares / jnp.sqrt(row_power[:, None] / (SIDE * SIDE) + 1e-06)).astype(jnp.bfloat16)
    return (refreshed, evidence)


def solution(mesh):
    assert mesh.devices.shape == (16, 32)
    fine = Mesh(mesh.devices.reshape(2, 4, 2, 2, 16), ALL)
    in_specs = (
        P(ALL, None),
        P(ALL),
        P(ALL, None),
        P(),
        P(REF, None),
    )
    out_specs = (P(REF, DOM), P(ALL))
    return jax.shard_map(
        per_device, mesh=fine, in_specs=in_specs, out_specs=out_specs, check_vma=False
    )
```

```python
import jax
import jax.numpy as jnp
from jax import lax
from jax.sharding import Mesh
from jax.sharding import PartitionSpec as P

SIDE = 64
REF = ("yh", "x", "c")
DOM = ("yl", "z")
ALL = REF + DOM
HALVING = (
    ("c", 2, 1),
    ("yl", 2, 1),
    ("x", 4, 1),
    ("yh", 2, 1),
    ("x", 4, 2),
)


def shift_matrices(moves):
    line = jnp.arange(SIDE, dtype=jnp.int32)
    source = jnp.mod(line[None, :, None] - moves[:, None, None], SIDE)
    return (line[None, None, :] == source).astype(jnp.bfloat16)


def roll_set(images, offsets, sign):
    grid = images.reshape(images.shape[0], SIDE, SIDE)
    rows = shift_matrices(sign * offsets[:, 0])
    cols = shift_matrices(sign * offsets[:, 1])
    moved = jnp.einsum("sai,nij->snaj", rows, grid, preferred_element_type=jnp.float32).astype(jnp.bfloat16)
    moved = jnp.einsum("snaj,sbj->snab", moved, cols, preferred_element_type=jnp.float32).astype(jnp.bfloat16)
    return moved.reshape(offsets.shape[0], images.shape[0], SIDE * SIDE)


def partner(axis, size, bit):
    return [(i, i ^ bit) for i in range(size)]


def reduce_blocks(partial):
    t = partial.reshape(2, 2, 2, 2, 8, 2, 2, 2, 2, 2, 128)
    t = t.transpose(3, 5, 2, 0, 1, 6, 7, 8, 9, 4, 10)
    for axis, size, bit in HALVING:
        mine = (lax.axis_index(axis) // bit) % 2
        keep = lax.dynamic_index_in_dim(t, mine, 0, keepdims=False)
        send = lax.dynamic_index_in_dim(t, 1 - mine, 0, keepdims=False)
        t = keep + lax.ppermute(send, axis, partner(axis, size, bit))
    t = t.reshape(-1, *t.shape[-2:])
    return jnp.sum(lax.all_to_all(t, "z", 0, 0, tiled=True), axis=0)


def gather_rows(rows):
    copies = jnp.broadcast_to(rows[None], (16, *rows.shape))
    return lax.all_to_all(copies, REF, 0, 0, tiled=True).reshape(-1, rows.shape[1])


def per_device(particles, inv_noise, candidates, offsets, references):
    tile_size = references.shape[0]
    all_classes = tile_size * 16
    stacked = roll_set(particles, offsets, -1)
    tile_rows = gather_rows(references)
    tile_float = tile_rows.astype(jnp.float32)
    norms = jnp.sum(tile_float * tile_float, axis=1)
    match_score = jnp.einsum(
        "spi,ji->psj", stacked, tile_rows, preferred_element_type=jnp.float32
    )
    update = match_score - 0.5 * norms[None, None, :]
    score = inv_noise[:, None, None] * update
    classes = jnp.arange(all_classes, dtype=jnp.int32)
    permitted_mask = jnp.any(candidates[:, :, None] == classes[None, None, :], axis=1)
    masked = jnp.where(permitted_mask[:, None, :], score, -1e30)
    peak_val = jnp.max(masked, axis=(1, 2))
    denom_sum = jnp.sum(jnp.exp(masked - peak_val[:, None, None]), axis=(1, 2))
    evidence = peak_val + jnp.log(denom_sum)
    weight = jnp.where(
        permitted_mask[:, None, :], jnp.exp(masked - evidence[:, None, None]), 0.0
    ).astype(jnp.bfloat16)
    partial = jnp.einsum("psk,spq->kq", weight, stacked, preferred_element_type=jnp.float32)
    shares = reduce_blocks(partial)
    row_power = jnp.sum(shares * shares, axis=1)
    row_power = row_power + lax.ppermute(row_power, "yl", partner("yl", 2, 1))
    row_power = jnp.broadcast_to(row_power[None], (16, row_power.shape[0]))
    row_power = jnp.sum(lax.all_to_all(row_power, "z", 0, 0, tiled=True), axis=0)
    refreshed = (shares / jnp.sqrt(row_power[:, None] / (SIDE * SIDE) + 1e-06)).astype(jnp.bfloat16)
    return (refreshed, evidence)


def solution(mesh):
    assert mesh.devices.shape == (16, 32)
    fine = Mesh(mesh.devices.reshape(2, 4, 2, 2, 16), ALL)
    in_specs = (
        P(ALL, None),
        P(ALL),
        P(ALL, None),
        P(),
        P(REF, None),
    )
    out_specs = (P(REF, DOM), P(ALL))
    return jax.shard_map(
        per_device, mesh=fine, in_specs=in_specs, out_specs=out_specs, check_vma=False
    )
```

```python
import jax
import jax.numpy as jnp
from jax import lax
from jax.sharding import Mesh
from jax.sharding import PartitionSpec as P

SIDE = 64
REF = ("yh", "x", "c")
DOM = ("yl", "z")
ALL = REF + DOM


def shift_matrices(moves):
    line = jnp.arange(SIDE, dtype=jnp.int32)
    source = jnp.mod(line[None, :, None] - moves[:, None, None], SIDE)
    return (line[None, None, :] == source).astype(jnp.bfloat16)


def roll_set(images, offsets, sign):
    grid = images.reshape(images.shape[0], SIDE, SIDE)
    rows = shift_matrices(sign * offsets[:, 0])
    cols = shift_matrices(sign * offsets[:, 1])
    moved = jnp.einsum("sai,nij->snaj", rows, grid, preferred_element_type=jnp.float32).astype(jnp.bfloat16)
    moved = jnp.einsum("snaj,sbj->snab", moved, cols, preferred_element_type=jnp.float32).astype(jnp.bfloat16)
    return moved.reshape(offsets.shape[0], images.shape[0], SIDE * SIDE)


def partner(axis, size, bit):
    return [(i, i ^ bit) for i in range(size)]


def halve(t, axis, size, bit, dim):
    mine = (lax.axis_index(axis) // bit) % 2
    keep = lax.dynamic_index_in_dim(t, mine, dim, keepdims=False)
    send = lax.dynamic_index_in_dim(t, 1 - mine, dim, keepdims=False)
    return keep + lax.ppermute(send, axis, partner(axis, size, bit))


def halve_pair(t, first, second):
    mid = t.shape[2] // 2
    a = halve(halve(lax.slice_in_dim(t, 0, mid, axis=2), *first, 0), *second, 0)
    b = halve(halve(lax.slice_in_dim(t, mid, t.shape[2], axis=2), *second, 1), *first, 0)
    return jnp.concatenate([a, b], axis=0)


def reduce_blocks(partial):
    t = partial.reshape(2, 2, 2, 2, 8, 2, 16, 128)
    t = t.transpose(3, 5, 2, 0, 1, 6, 4, 7)
    t = halve(t, "c", 2, 1, 0)
    t = halve_pair(t, ("yl", 2, 1), ("x", 4, 1))
    t = halve_pair(t, ("yh", 2, 1), ("x", 4, 2))
    return jnp.sum(lax.all_to_all(t, "z", 0, 0, tiled=True), axis=0)


def gather_rows(rows):
    copies = jnp.broadcast_to(rows[None], (16, *rows.shape))
    return lax.all_to_all(copies, REF, 0, 0, tiled=True).reshape(-1, rows.shape[1])


def per_device(particles, inv_noise, candidates, offsets, references):
    tile_size = references.shape[0]
    all_classes = tile_size * 16
    stacked = roll_set(particles, offsets, -1)
    tile_rows = gather_rows(references)
    tile_float = tile_rows.astype(jnp.float32)
    norms = jnp.sum(tile_float * tile_float, axis=1)
    match_score = jnp.einsum(
        "spi,ji->psj", stacked, tile_rows, preferred_element_type=jnp.float32
    )
    update = match_score - 0.5 * norms[None, None, :]
    score = inv_noise[:, None, None] * update
    classes = jnp.arange(all_classes, dtype=jnp.int32)
    permitted_mask = jnp.any(candidates[:, :, None] == classes[None, None, :], axis=1)
    masked = jnp.where(permitted_mask[:, None, :], score, -1e30)
    peak_val = jnp.max(masked, axis=(1, 2))
    denom_sum = jnp.sum(jnp.exp(masked - peak_val[:, None, None]), axis=(1, 2))
    evidence = peak_val + jnp.log(denom_sum)
    weight = jnp.where(
        permitted_mask[:, None, :], jnp.exp(masked - evidence[:, None, None]), 0.0
    ).astype(jnp.bfloat16)
    partial = jnp.einsum("psk,spq->kq", weight, stacked, preferred_element_type=jnp.float32)
    shares = reduce_blocks(partial)
    row_power = jnp.sum(shares * shares, axis=1)
    row_power = row_power + lax.ppermute(row_power, "yl", partner("yl", 2, 1))
    row_power = jnp.broadcast_to(row_power[None], (16, row_power.shape[0]))
    row_power = jnp.sum(lax.all_to_all(row_power, "z", 0, 0, tiled=True), axis=0)
    refreshed = (shares / jnp.sqrt(row_power[:, None] / (SIDE * SIDE) + 1e-06)).astype(jnp.bfloat16)
    return (refreshed, evidence)


def solution(mesh):
    assert mesh.devices.shape == (16, 32)
    fine = Mesh(mesh.devices.reshape(2, 4, 2, 2, 16), ALL)
    in_specs = (
        P(ALL, None),
        P(ALL),
        P(ALL, None),
        P(),
        P(REF, None),
    )
    out_specs = (P(REF, DOM), P(ALL))
    return jax.shard_map(
        per_device, mesh=fine, in_specs=in_specs, out_specs=out_specs, check_vma=False
    )
```

```python
import jax
import jax.numpy as jnp
from jax import lax
from jax.sharding import Mesh
from jax.sharding import PartitionSpec as P

SIDE = 64
REF = ("yh", "x", "c")
DOM = ("yl", "z")
ALL = REF + DOM
SPREAD = ("yh", "x", "yl", "z")


def shift_matrices(moves):
    line = jnp.arange(SIDE, dtype=jnp.int32)
    source = jnp.mod(line[None, :, None] - moves[:, None, None], SIDE)
    return (line[None, None, :] == source).astype(jnp.bfloat16)


def roll_set(images, offsets, sign):
    grid = images.reshape(images.shape[0], SIDE, SIDE)
    rows = shift_matrices(sign * offsets[:, 0])
    cols = shift_matrices(sign * offsets[:, 1])
    moved = jnp.einsum("sai,nij->snaj", rows, grid, preferred_element_type=jnp.float32).astype(jnp.bfloat16)
    moved = jnp.einsum("snaj,sbj->snab", moved, cols, preferred_element_type=jnp.float32).astype(jnp.bfloat16)
    return moved.reshape(offsets.shape[0], images.shape[0], SIDE * SIDE)


def partner(axis, size, bit):
    return [(i, i ^ bit) for i in range(size)]


def halve(t, axis, size, bit, dim):
    mine = (lax.axis_index(axis) // bit) % 2
    keep = lax.dynamic_index_in_dim(t, mine, dim, keepdims=False)
    send = lax.dynamic_index_in_dim(t, 1 - mine, dim, keepdims=False)
    return keep + lax.ppermute(send, axis, partner(axis, size, bit))


def halve_pair(t, first, second):
    mid = t.shape[2] // 2
    a = halve(halve(lax.slice_in_dim(t, 0, mid, axis=2), *first, 0), *second, 0)
    b = halve(halve(lax.slice_in_dim(t, mid, t.shape[2], axis=2), *second, 1), *first, 0)
    return jnp.concatenate([a, b], axis=0)


def reduce_blocks(partial):
    t = partial.reshape(2, 2, 2, 2, 8, 2, 16, 128)
    t = t.transpose(3, 0, 1, 2, 5, 6, 4, 7)
    t = halve(t, "c", 2, 1, 0)
    t = t.reshape(-1, *t.shape[-2:])
    return jnp.sum(lax.all_to_all(t, SPREAD, 0, 0, tiled=True), axis=0)


def gather_rows(rows):
    copies = jnp.broadcast_to(rows[None], (16, *rows.shape))
    return lax.all_to_all(copies, REF, 0, 0, tiled=True).reshape(-1, rows.shape[1])


def per_device(particles, inv_noise, candidates, offsets, references):
    tile_size = references.shape[0]
    all_classes = tile_size * 16
    stacked = roll_set(particles, offsets, -1)
    tile_rows = gather_rows(references)
    tile_float = tile_rows.astype(jnp.float32)
    norms = jnp.sum(tile_float * tile_float, axis=1)
    match_score = jnp.einsum(
        "spi,ji->psj", stacked, tile_rows, preferred_element_type=jnp.float32
    )
    update = match_score - 0.5 * norms[None, None, :]
    score = inv_noise[:, None, None] * update
    classes = jnp.arange(all_classes, dtype=jnp.int32)
    permitted_mask = jnp.any(candidates[:, :, None] == classes[None, None, :], axis=1)
    masked = jnp.where(permitted_mask[:, None, :], score, -1e30)
    peak_val = jnp.max(masked, axis=(1, 2))
    denom_sum = jnp.sum(jnp.exp(masked - peak_val[:, None, None]), axis=(1, 2))
    evidence = peak_val + jnp.log(denom_sum)
    weight = jnp.where(
        permitted_mask[:, None, :], jnp.exp(masked - evidence[:, None, None]), 0.0
    ).astype(jnp.bfloat16)
    partial = jnp.einsum("psk,spq->kq", weight, stacked, preferred_element_type=jnp.float32)
    shares = reduce_blocks(partial)
    row_power = jnp.sum(shares * shares, axis=1)
    row_power = jnp.broadcast_to(row_power[None], (32, row_power.shape[0]))
    row_power = jnp.sum(lax.all_to_all(row_power, DOM, 0, 0, tiled=True), axis=0)
    refreshed = (shares / jnp.sqrt(row_power[:, None] / (SIDE * SIDE) + 1e-06)).astype(jnp.bfloat16)
    return (refreshed, evidence)


def solution(mesh):
    assert mesh.devices.shape == (16, 32)
    fine = Mesh(mesh.devices.reshape(2, 4, 2, 2, 16), ALL)
    in_specs = (
        P(ALL, None),
        P(ALL),
        P(ALL, None),
        P(),
        P(REF, None),
    )
    out_specs = (P(REF, DOM), P(ALL))
    return jax.shard_map(
        per_device, mesh=fine, in_specs=in_specs, out_specs=out_specs, check_vma=False
    )
```

```python
import jax
import jax.numpy as jnp
from jax import lax
from jax.sharding import Mesh
from jax.sharding import PartitionSpec as P

SIDE = 64
REF = ("yh", "x", "c")
DOM = ("yl", "z")
ALL = REF + DOM


def roll_set(images, offsets, sign):
    n = images.shape[0]
    grid = images.reshape(n, SIDE // 2, 2 * SIDE)
    row_move = sign * offsets[:, 0]
    col_move = sign * offsets[:, 1]
    half = jnp.arange(2, dtype=jnp.int32)
    to_half = jnp.mod(half[None, :] + row_move[:, None], 2)
    to_row = (half[None, :] + row_move[:, None] - to_half) // 2
    lane = jnp.arange(2 * SIDE, dtype=jnp.int32)
    lane_half, column = lane // SIDE, lane % SIDE
    moved_column = jnp.mod(column[None, :] + col_move[:, None], SIDE)
    lanes = (
        (lane_half[None, None, :, None] == half[None, :, None, None])
        & (lane_half[None, None, None, :] == to_half[:, :, None, None])
        & (column[None, None, None, :] == moved_column[:, None, :, None])
    ).astype(jnp.bfloat16)
    line = jnp.arange(SIDE // 2, dtype=jnp.int32)
    rows = (
        line[None, None, None, :] == jnp.mod(line[None, None, :, None] - to_row[:, :, None, None], SIDE // 2)
    ).astype(jnp.bfloat16)
    moved = jnp.einsum("nrl,shlm->shnrm", grid, lanes, preferred_element_type=jnp.float32).astype(jnp.bfloat16)
    return jnp.einsum("shqr,shnrm->snqm", rows, moved, preferred_element_type=jnp.float32).astype(jnp.bfloat16)


def partner(axis, size, bit):
    return [(i, i ^ bit) for i in range(size)]


def halve(t, axis, size, bit, dim):
    mine = (lax.axis_index(axis) // bit) % 2
    keep = lax.dynamic_index_in_dim(t, mine, dim, keepdims=False)
    send = lax.dynamic_index_in_dim(t, 1 - mine, dim, keepdims=False)
    return keep + lax.ppermute(send, axis, partner(axis, size, bit))


def halve_pair(t, first, second):
    mid = t.shape[2] // 2
    a = halve(halve(lax.slice_in_dim(t, 0, mid, axis=2), *first, 0), *second, 0)
    b = halve(halve(lax.slice_in_dim(t, mid, t.shape[2], axis=2), *second, 1), *first, 0)
    return jnp.concatenate([a, b], axis=0)


def reduce_blocks(partial):
    t = partial.reshape(2, 2, 2, 2, 8, 2, 16, 128)
    t = t.transpose(3, 5, 2, 0, 1, 6, 4, 7)
    t = halve(t, "c", 2, 1, 0)
    t = halve_pair(t, ("yl", 2, 1), ("x", 4, 1))
    t = halve_pair(t, ("yh", 2, 1), ("x", 4, 2))
    return jnp.sum(lax.all_to_all(t, "z", 0, 0, tiled=True), axis=0)


def gather_rows(rows):
    copies = jnp.broadcast_to(rows[None], (16, *rows.shape))
    return lax.all_to_all(copies, REF, 0, 0, tiled=True).reshape(-1, rows.shape[1])


def per_device(particles, inv_noise, candidates, offsets, references):
    tile_size = references.shape[0]
    all_classes = tile_size * 16
    stacked = roll_set(particles, offsets, -1)
    tile_rows = gather_rows(references)
    tile_float = tile_rows.astype(jnp.float32)
    norms = jnp.sum(tile_float * tile_float, axis=1)
    match_score = jnp.einsum(
        "sprl,jrl->psj", stacked, tile_rows.reshape(tile_rows.shape[0], *stacked.shape[2:]),
        preferred_element_type=jnp.float32,
    )
    update = match_score - 0.5 * norms[None, None, :]
    score = inv_noise[:, None, None] * update
    classes = jnp.arange(all_classes, dtype=jnp.int32)
    permitted_mask = jnp.any(candidates[:, :, None] == classes[None, None, :], axis=1)
    masked = jnp.where(permitted_mask[:, None, :], score, -1e30)
    peak_val = jnp.max(masked, axis=(1, 2))
    denom_sum = jnp.sum(jnp.exp(masked - peak_val[:, None, None]), axis=(1, 2))
    evidence = peak_val + jnp.log(denom_sum)
    weight = jnp.where(
        permitted_mask[:, None, :], jnp.exp(masked - evidence[:, None, None]), 0.0
    ).astype(jnp.bfloat16)
    partial = jnp.einsum("psk,sprl->krl", weight, stacked, preferred_element_type=jnp.float32)
    shares = reduce_blocks(partial)
    row_power = jnp.sum(shares * shares, axis=1)
    row_power = row_power + lax.ppermute(row_power, "yl", partner("yl", 2, 1))
    row_power = jnp.broadcast_to(row_power[None], (16, row_power.shape[0]))
    row_power = jnp.sum(lax.all_to_all(row_power, "z", 0, 0, tiled=True), axis=0)
    refreshed = (shares / jnp.sqrt(row_power[:, None] / (SIDE * SIDE) + 1e-06)).astype(jnp.bfloat16)
    return (refreshed, evidence)


def solution(mesh):
    assert mesh.devices.shape == (16, 32)
    fine = Mesh(mesh.devices.reshape(2, 4, 2, 2, 16), ALL)
    in_specs = (
        P(ALL, None),
        P(ALL),
        P(ALL, None),
        P(),
        P(REF, None),
    )
    out_specs = (P(REF, DOM), P(ALL))
    return jax.shard_map(
        per_device, mesh=fine, in_specs=in_specs, out_specs=out_specs, check_vma=False
    )
```

```python
import jax
import jax.numpy as jnp
from jax import lax
from jax.sharding import Mesh
from jax.sharding import PartitionSpec as P

SIDE = 64
REF = ("yh", "x", "c")
DOM = ("yl", "z")
ALL = REF + DOM
PLANE = ("yh", "x", "yl")


def shift_matrices(moves):
    line = jnp.arange(SIDE, dtype=jnp.int32)
    source = jnp.mod(line[None, :, None] - moves[:, None, None], SIDE)
    return (line[None, None, :] == source).astype(jnp.bfloat16)


def roll_set(images, offsets, sign):
    grid = images.reshape(images.shape[0], SIDE, SIDE)
    rows = shift_matrices(sign * offsets[:, 0])
    cols = shift_matrices(sign * offsets[:, 1])
    moved = jnp.einsum("sai,nij->snaj", rows, grid, preferred_element_type=jnp.float32).astype(jnp.bfloat16)
    moved = jnp.einsum("snaj,sbj->snab", moved, cols, preferred_element_type=jnp.float32).astype(jnp.bfloat16)
    return moved.reshape(offsets.shape[0], images.shape[0], SIDE * SIDE)


def partner(axis, size, bit):
    return [(i, i ^ bit) for i in range(size)]


def halve(t, axis, size, bit, dim):
    mine = (lax.axis_index(axis) // bit) % 2
    keep = lax.dynamic_index_in_dim(t, mine, dim, keepdims=False)
    send = lax.dynamic_index_in_dim(t, 1 - mine, dim, keepdims=False)
    return keep + lax.ppermute(send, axis, partner(axis, size, bit))


def halve_pair(t, first, second):
    mid = t.shape[2] // 2
    a = halve(halve(lax.slice_in_dim(t, 0, mid, axis=2), *first, 0), *second, 0)
    b = halve(halve(lax.slice_in_dim(t, mid, t.shape[2], axis=2), *second, 1), *first, 0)
    return jnp.concatenate([a, b], axis=0)


def reduce_blocks(partial):
    t = partial.reshape(2, 2, 2, 2, 8, 2, 16, 128)
    t = t.transpose(3, 0, 1, 2, 5, 6, 4, 7)
    t = halve(t, "c", 2, 1, 0)
    t = t.reshape(-1, *t.shape[-3:])
    t = jnp.sum(lax.all_to_all(t, PLANE, 0, 0, tiled=True), axis=0)
    return jnp.sum(lax.all_to_all(t, "z", 0, 0, tiled=True), axis=0)


def gather_rows(rows):
    copies = jnp.broadcast_to(rows[None], (16, *rows.shape))
    return lax.all_to_all(copies, REF, 0, 0, tiled=True).reshape(-1, rows.shape[1])


def per_device(particles, inv_noise, candidates, offsets, references):
    tile_size = references.shape[0]
    all_classes = tile_size * 16
    stacked = roll_set(particles, offsets, -1)
    tile_rows = gather_rows(references)
    tile_float = tile_rows.astype(jnp.float32)
    norms = jnp.sum(tile_float * tile_float, axis=1)
    match_score = jnp.einsum(
        "spi,ji->psj", stacked, tile_rows, preferred_element_type=jnp.float32
    )
    update = match_score - 0.5 * norms[None, None, :]
    score = inv_noise[:, None, None] * update
    classes = jnp.arange(all_classes, dtype=jnp.int32)
    permitted_mask = jnp.any(candidates[:, :, None] == classes[None, None, :], axis=1)
    masked = jnp.where(permitted_mask[:, None, :], score, -1e30)
    peak_val = jnp.max(masked, axis=(1, 2))
    denom_sum = jnp.sum(jnp.exp(masked - peak_val[:, None, None]), axis=(1, 2))
    evidence = peak_val + jnp.log(denom_sum)
    weight = jnp.where(
        permitted_mask[:, None, :], jnp.exp(masked - evidence[:, None, None]), 0.0
    ).astype(jnp.bfloat16)
    partial = jnp.einsum("psk,spq->kq", weight, stacked, preferred_element_type=jnp.float32)
    shares = reduce_blocks(partial)
    row_power = jnp.sum(shares * shares, axis=1)
    row_power = row_power + lax.ppermute(row_power, "yl", partner("yl", 2, 1))
    row_power = jnp.broadcast_to(row_power[None], (16, row_power.shape[0]))
    row_power = jnp.sum(lax.all_to_all(row_power, "z", 0, 0, tiled=True), axis=0)
    refreshed = (shares / jnp.sqrt(row_power[:, None] / (SIDE * SIDE) + 1e-06)).astype(jnp.bfloat16)
    return (refreshed, evidence)


def solution(mesh):
    assert mesh.devices.shape == (16, 32)
    fine = Mesh(mesh.devices.reshape(2, 4, 2, 2, 16), ALL)
    in_specs = (
        P(ALL, None),
        P(ALL),
        P(ALL, None),
        P(),
        P(REF, None),
    )
    out_specs = (P(REF, DOM), P(ALL))
    return jax.shard_map(
        per_device, mesh=fine, in_specs=in_specs, out_specs=out_specs, check_vma=False
    )
```

```python
import jax
import jax.numpy as jnp
from jax import lax
from jax.sharding import Mesh
from jax.sharding import PartitionSpec as P

SIDE = 64
REF = ("yh", "x", "c")
DOM = ("yl", "z")
ALL = REF + DOM
PLANE = ("yh", "x", "c", "yl")


def shift_matrices(moves):
    line = jnp.arange(SIDE, dtype=jnp.int32)
    source = jnp.mod(line[None, :, None] - moves[:, None, None], SIDE)
    return (line[None, None, :] == source).astype(jnp.bfloat16)


def roll_set(images, offsets, sign):
    grid = images.reshape(images.shape[0], SIDE, SIDE)
    rows = shift_matrices(sign * offsets[:, 0])
    cols = shift_matrices(sign * offsets[:, 1])
    moved = jnp.einsum("sai,nij->snaj", rows, grid, preferred_element_type=jnp.float32).astype(jnp.bfloat16)
    moved = jnp.einsum("snaj,sbj->snab", moved, cols, preferred_element_type=jnp.float32).astype(jnp.bfloat16)
    return moved.reshape(offsets.shape[0], images.shape[0], SIDE * SIDE)


def partner(axis, size, bit):
    return [(i, i ^ bit) for i in range(size)]


def halve(t, axis, size, bit, dim):
    mine = (lax.axis_index(axis) // bit) % 2
    keep = lax.dynamic_index_in_dim(t, mine, dim, keepdims=False)
    send = lax.dynamic_index_in_dim(t, 1 - mine, dim, keepdims=False)
    return keep + lax.ppermute(send, axis, partner(axis, size, bit))


def halve_pair(t, first, second):
    mid = t.shape[2] // 2
    a = halve(halve(lax.slice_in_dim(t, 0, mid, axis=2), *first, 0), *second, 0)
    b = halve(halve(lax.slice_in_dim(t, mid, t.shape[2], axis=2), *second, 1), *first, 0)
    return jnp.concatenate([a, b], axis=0)


def reduce_blocks(partial):
    t = partial.reshape(2, 2, 2, 2, 8, 2, 16, 128)
    t = t.transpose(0, 1, 2, 3, 5, 6, 4, 7)
    t = t.reshape(-1, *t.shape[-3:])
    t = jnp.sum(lax.all_to_all(t, PLANE, 0, 0, tiled=True), axis=0)
    return jnp.sum(lax.all_to_all(t, "z", 0, 0, tiled=True), axis=0)


def gather_rows(rows):
    copies = jnp.broadcast_to(rows[None], (16, *rows.shape))
    return lax.all_to_all(copies, REF, 0, 0, tiled=True).reshape(-1, rows.shape[1])


def per_device(particles, inv_noise, candidates, offsets, references):
    tile_size = references.shape[0]
    all_classes = tile_size * 16
    stacked = roll_set(particles, offsets, -1)
    tile_rows = gather_rows(references)
    tile_float = tile_rows.astype(jnp.float32)
    norms = jnp.sum(tile_float * tile_float, axis=1)
    match_score = jnp.einsum(
        "spi,ji->psj", stacked, tile_rows, preferred_element_type=jnp.float32
    )
    update = match_score - 0.5 * norms[None, None, :]
    score = inv_noise[:, None, None] * update
    classes = jnp.arange(all_classes, dtype=jnp.int32)
    permitted_mask = jnp.any(candidates[:, :, None] == classes[None, None, :], axis=1)
    masked = jnp.where(permitted_mask[:, None, :], score, -1e30)
    peak_val = jnp.max(masked, axis=(1, 2))
    denom_sum = jnp.sum(jnp.exp(masked - peak_val[:, None, None]), axis=(1, 2))
    evidence = peak_val + jnp.log(denom_sum)
    weight = jnp.where(
        permitted_mask[:, None, :], jnp.exp(masked - evidence[:, None, None]), 0.0
    ).astype(jnp.bfloat16)
    partial = jnp.einsum("psk,spq->kq", weight, stacked, preferred_element_type=jnp.float32)
    shares = reduce_blocks(partial)
    row_power = jnp.sum(shares * shares, axis=1)
    row_power = row_power + lax.ppermute(row_power, "yl", partner("yl", 2, 1))
    row_power = jnp.broadcast_to(row_power[None], (16, row_power.shape[0]))
    row_power = jnp.sum(lax.all_to_all(row_power, "z", 0, 0, tiled=True), axis=0)
    refreshed = (shares / jnp.sqrt(row_power[:, None] / (SIDE * SIDE) + 1e-06)).astype(jnp.bfloat16)
    return (refreshed, evidence)


def solution(mesh):
    assert mesh.devices.shape == (16, 32)
    fine = Mesh(mesh.devices.reshape(2, 4, 2, 2, 16), ALL)
    in_specs = (
        P(ALL, None),
        P(ALL),
        P(ALL, None),
        P(),
        P(REF, None),
    )
    out_specs = (P(REF, DOM), P(ALL))
    return jax.shard_map(
        per_device, mesh=fine, in_specs=in_specs, out_specs=out_specs, check_vma=False
    )
```

```python
import jax
import jax.numpy as jnp
from jax import lax
from jax.sharding import Mesh
from jax.sharding import PartitionSpec as P

SIDE = 64
REF = ("yh", "x", "c")
DOM = ("yl", "z")
ALL = REF + DOM
PLANE = ("yh", "x", "yl")


def shift_matrices(moves):
    line = jnp.arange(SIDE, dtype=jnp.int32)
    source = jnp.mod(line[None, :, None] - moves[:, None, None], SIDE)
    return (line[None, None, :] == source).astype(jnp.bfloat16)


def roll_set(images, offsets, sign):
    grid = images.reshape(images.shape[0], SIDE, SIDE)
    rows = shift_matrices(sign * offsets[:, 0])
    cols = shift_matrices(sign * offsets[:, 1])
    moved = jnp.einsum("sai,nij->snaj", rows, grid, preferred_element_type=jnp.float32).astype(jnp.bfloat16)
    moved = jnp.einsum("snaj,sbj->snab", moved, cols, preferred_element_type=jnp.float32).astype(jnp.bfloat16)
    return moved.reshape(offsets.shape[0], images.shape[0], SIDE * SIDE)


def partner(axis, size, bit):
    return [(i, i ^ bit) for i in range(size)]


def halve(t, axis, size, bit, dim):
    mine = (lax.axis_index(axis) // bit) % 2
    keep = lax.dynamic_index_in_dim(t, mine, dim, keepdims=False)
    send = lax.dynamic_index_in_dim(t, 1 - mine, dim, keepdims=False)
    return keep + lax.ppermute(send, axis, partner(axis, size, bit))


def halve_pair(t, first, second):
    mid = t.shape[2] // 2
    a = halve(halve(lax.slice_in_dim(t, 0, mid, axis=2), *first, 0), *second, 0)
    b = halve(halve(lax.slice_in_dim(t, mid, t.shape[2], axis=2), *second, 1), *first, 0)
    return jnp.concatenate([a, b], axis=0)


def reduce_blocks(partial):
    t = partial.reshape(2, 2, 2, 2, 8, 2, 16, 128)
    t = t.transpose(3, 0, 1, 2, 5, 6, 4, 7)
    t = halve(t, "c", 2, 1, 0)
    t = t.reshape(-1, *t.shape[-3:])
    t = jnp.sum(lax.all_to_all(t, PLANE, 0, 0, tiled=True), axis=0)
    return jnp.sum(lax.all_to_all(t, "z", 0, 0, tiled=True), axis=0)


def gather_rows(rows):
    copies = jnp.broadcast_to(rows[None], (8, *rows.shape))
    mine = lax.all_to_all(copies, ("yh", "x"), 0, 0, tiled=True)
    other = lax.ppermute(mine, "c", partner("c", 2, 1))
    first = lax.axis_index("c") == 0
    both = jnp.stack([jnp.where(first, mine, other), jnp.where(first, other, mine)], axis=1)
    return both.reshape(-1, rows.shape[1])


def per_device(particles, inv_noise, candidates, offsets, references):
    tile_size = references.shape[0]
    all_classes = tile_size * 16
    stacked = roll_set(particles, offsets, -1)
    tile_rows = gather_rows(references)
    tile_float = tile_rows.astype(jnp.float32)
    norms = jnp.sum(tile_float * tile_float, axis=1)
    match_score = jnp.einsum(
        "spi,ji->psj", stacked, tile_rows, preferred_element_type=jnp.float32
    )
    update = match_score - 0.5 * norms[None, None, :]
    score = inv_noise[:, None, None] * update
    classes = jnp.arange(all_classes, dtype=jnp.int32)
    permitted_mask = jnp.any(candidates[:, :, None] == classes[None, None, :], axis=1)
    masked = jnp.where(permitted_mask[:, None, :], score, -1e30)
    peak_val = jnp.max(masked, axis=(1, 2))
    denom_sum = jnp.sum(jnp.exp(masked - peak_val[:, None, None]), axis=(1, 2))
    evidence = peak_val + jnp.log(denom_sum)
    weight = jnp.where(
        permitted_mask[:, None, :], jnp.exp(masked - evidence[:, None, None]), 0.0
    ).astype(jnp.bfloat16)
    partial = jnp.einsum("psk,spq->kq", weight, stacked, preferred_element_type=jnp.float32)
    shares = reduce_blocks(partial)
    row_power = jnp.sum(shares * shares, axis=1)
    row_power = row_power + lax.ppermute(row_power, "yl", partner("yl", 2, 1))
    row_power = jnp.broadcast_to(row_power[None], (16, row_power.shape[0]))
    row_power = jnp.sum(lax.all_to_all(row_power, "z", 0, 0, tiled=True), axis=0)
    refreshed = (shares / jnp.sqrt(row_power[:, None] / (SIDE * SIDE) + 1e-06)).astype(jnp.bfloat16)
    return (refreshed, evidence)


def solution(mesh):
    assert mesh.devices.shape == (16, 32)
    fine = Mesh(mesh.devices.reshape(2, 4, 2, 2, 16), ALL)
    in_specs = (
        P(ALL, None),
        P(ALL),
        P(ALL, None),
        P(),
        P(REF, None),
    )
    out_specs = (P(REF, DOM), P(ALL))
    return jax.shard_map(
        per_device, mesh=fine, in_specs=in_specs, out_specs=out_specs, check_vma=False
    )
```

```python
import jax
import jax.numpy as jnp
from jax import lax
from jax.sharding import Mesh
from jax.sharding import PartitionSpec as P

SIDE = 64
REF = ("yh", "x", "c")
DOM = ("yl", "z")
ALL = REF + DOM
PLANE = ("yh", "x", "yl")


def shift_matrices(moves):
    line = jnp.arange(SIDE, dtype=jnp.int32)
    source = jnp.mod(line[None, :, None] - moves[:, None, None], SIDE)
    return (line[None, None, :] == source).astype(jnp.bfloat16)


def roll_set(images, offsets, sign):
    grid = images.reshape(images.shape[0], SIDE, SIDE)
    rows = shift_matrices(sign * offsets[:, 0])
    cols = shift_matrices(sign * offsets[:, 1])
    moved = jnp.einsum("sai,nij->snaj", rows, grid, preferred_element_type=jnp.float32).astype(jnp.bfloat16)
    moved = jnp.einsum("snaj,sbj->snab", moved, cols, preferred_element_type=jnp.float32).astype(jnp.bfloat16)
    return moved.reshape(offsets.shape[0], images.shape[0], SIDE * SIDE)


def partner(size, bit):
    return [(i, i ^ bit) for i in range(size)]


def halve(t, axis, size, bit, dim):
    mine = (lax.axis_index(axis) // bit) % 2
    keep = lax.dynamic_index_in_dim(t, mine, dim, keepdims=False)
    send = lax.dynamic_index_in_dim(t, 1 - mine, dim, keepdims=False)
    return keep + lax.ppermute(send, axis, partner(size, bit))


def reduce_blocks(partial):
    t = partial.reshape(2, 2, 2, 2, 8, 2, 16, 128)
    t = t.transpose(3, 0, 1, 2, 5, 6, 4, 7)
    t = halve(t, "c", 2, 1, 0)
    t = t.reshape(-1, *t.shape[-3:])
    t = jnp.sum(lax.all_to_all(t, PLANE, 0, 0, tiled=True), axis=0)
    return jnp.sum(lax.all_to_all(t, "z", 0, 0, tiled=True), axis=0)


def gather_rows(rows):
    copies = jnp.broadcast_to(rows[None], (8, *rows.shape))
    mine = lax.all_to_all(copies, ("yh", "x"), 0, 0, tiled=True)
    other = lax.ppermute(mine, "c", partner(2, 1))
    first = lax.axis_index("c") == 0
    both = jnp.stack([jnp.where(first, mine, other), jnp.where(first, other, mine)], axis=1)
    return both.reshape(-1, rows.shape[1])


def step(particles, inv_noise, candidates, offsets, references):
    tile_size = references.shape[0]
    all_classes = tile_size * 16
    stacked = roll_set(particles, offsets, -1)
    tile_rows = gather_rows(references)
    tile_float = tile_rows.astype(jnp.float32)
    norms = jnp.sum(tile_float * tile_float, axis=1)
    match_score = jnp.einsum(
        "spi,ji->psj", stacked, tile_rows, preferred_element_type=jnp.float32
    )
    update = match_score - 0.5 * norms[None, None, :]
    score = inv_noise[:, None, None] * update
    classes = jnp.arange(all_classes, dtype=jnp.int32)
    permitted_mask = jnp.any(candidates[:, :, None] == classes[None, None, :], axis=1)
    masked = jnp.where(permitted_mask[:, None, :], score, -1e30)
    peak_val = jnp.max(masked, axis=(1, 2))
    denom_sum = jnp.sum(jnp.exp(masked - peak_val[:, None, None]), axis=(1, 2))
    evidence = peak_val + jnp.log(denom_sum)
    weight = jnp.where(
        permitted_mask[:, None, :], jnp.exp(masked - evidence[:, None, None]), 0.0
    ).astype(jnp.bfloat16)
    partial = jnp.einsum("psk,spq->kq", weight, stacked, preferred_element_type=jnp.float32)
    shares = reduce_blocks(partial)
    row_power = jnp.sum(shares * shares, axis=1)
    row_power = row_power + lax.ppermute(row_power, "yl", partner(2, 1))
    row_power = jnp.broadcast_to(row_power[None], (16, row_power.shape[0]))
    row_power = jnp.sum(lax.all_to_all(row_power, "z", 0, 0, tiled=True), axis=0)
    refreshed = (shares / jnp.sqrt(row_power[:, None] / (SIDE * SIDE) + 1e-06)).astype(jnp.bfloat16)
    return (refreshed, evidence)


def solution(mesh):
    assert mesh.devices.shape == (16, 32)
    fine = Mesh(mesh.devices.reshape(2, 4, 2, 2, 16), ALL)
    in_specs = (
        P(ALL, None),
        P(ALL),
        P(ALL, None),
        P(),
        P(REF, None),
    )
    out_specs = (P(REF, DOM), P(ALL))
    return jax.shard_map(step, mesh=fine, in_specs=in_specs, out_specs=out_specs, check_vma=False)
```

```python
import jax
import jax.numpy as jnp
from jax import lax
from jax.sharding import Mesh
from jax.sharding import PartitionSpec as P

SIDE = 64
REF = ("yh", "x", "c")
DOM = ("yl", "z")
ALL = REF + DOM
PLANE = ("yh", "x", "yl")


def shift_matrices(moves):
    line = jnp.arange(SIDE, dtype=jnp.int32)
    source = jnp.mod(line[None, :, None] - moves[:, None, None], SIDE)
    return (line[None, None, :] == source).astype(jnp.bfloat16)


def roll_set(images, offsets, sign):
    grid = images.reshape(images.shape[0], SIDE, SIDE)
    rows = shift_matrices(sign * offsets[:, 0])
    cols = shift_matrices(sign * offsets[:, 1])
    moved = jnp.einsum("sai,nij->snaj", rows, grid, preferred_element_type=jnp.float32).astype(jnp.bfloat16)
    moved = jnp.einsum("snaj,sbj->snab", moved, cols, preferred_element_type=jnp.float32).astype(jnp.bfloat16)
    return moved.reshape(offsets.shape[0], images.shape[0], SIDE * SIDE)


def partner(axis, size, bit):
    return [(i, i ^ bit) for i in range(size)]


def halve(t, axis, size, bit, dim):
    mine = (lax.axis_index(axis) // bit) % 2
    keep = lax.dynamic_index_in_dim(t, mine, dim, keepdims=False)
    send = lax.dynamic_index_in_dim(t, 1 - mine, dim, keepdims=False)
    return keep + lax.ppermute(send, axis, partner(axis, size, bit))


def halve_pair(t, first, second):
    mid = t.shape[2] // 2
    a = halve(halve(lax.slice_in_dim(t, 0, mid, axis=2), *first, 0), *second, 0)
    b = halve(halve(lax.slice_in_dim(t, mid, t.shape[2], axis=2), *second, 1), *first, 0)
    return jnp.concatenate([a, b], axis=0)


def reduce_blocks(partial):
    t = partial.reshape(2, 2, 2, 2, 8, 2, 16, 128)
    t = t.transpose(3, 6, 0, 1, 2, 5, 4, 7)
    t = halve(t, "c", 2, 1, 0)
    t = jnp.sum(lax.all_to_all(t, "z", 0, 0, tiled=True), axis=0)
    t = t.reshape(-1, *t.shape[-2:])
    return jnp.sum(lax.all_to_all(t, PLANE, 0, 0, tiled=True), axis=0)


def gather_rows(rows):
    copies = jnp.broadcast_to(rows[None], (16, *rows.shape))
    return lax.all_to_all(copies, REF, 0, 0, tiled=True).reshape(-1, rows.shape[1])


def per_device(particles, inv_noise, candidates, offsets, references):
    tile_size = references.shape[0]
    all_classes = tile_size * 16
    stacked = roll_set(particles, offsets, -1)
    tile_rows = gather_rows(references)
    tile_float = tile_rows.astype(jnp.float32)
    norms = jnp.sum(tile_float * tile_float, axis=1)
    match_score = jnp.einsum(
        "spi,ji->psj", stacked, tile_rows, preferred_element_type=jnp.float32
    )
    update = match_score - 0.5 * norms[None, None, :]
    score = inv_noise[:, None, None] * update
    classes = jnp.arange(all_classes, dtype=jnp.int32)
    permitted_mask = jnp.any(candidates[:, :, None] == classes[None, None, :], axis=1)
    masked = jnp.where(permitted_mask[:, None, :], score, -1e30)
    peak_val = jnp.max(masked, axis=(1, 2))
    denom_sum = jnp.sum(jnp.exp(masked - peak_val[:, None, None]), axis=(1, 2))
    evidence = peak_val + jnp.log(denom_sum)
    weight = jnp.where(
        permitted_mask[:, None, :], jnp.exp(masked - evidence[:, None, None]), 0.0
    ).astype(jnp.bfloat16)
    partial = jnp.einsum("psk,spq->kq", weight, stacked, preferred_element_type=jnp.float32)
    shares = reduce_blocks(partial)
    row_power = jnp.sum(shares * shares, axis=1)
    row_power = row_power + lax.ppermute(row_power, "yl", partner("yl", 2, 1))
    row_power = jnp.broadcast_to(row_power[None], (16, row_power.shape[0]))
    row_power = jnp.sum(lax.all_to_all(row_power, "z", 0, 0, tiled=True), axis=0)
    refreshed = (shares / jnp.sqrt(row_power[:, None] / (SIDE * SIDE) + 1e-06)).astype(jnp.bfloat16)
    return (refreshed, evidence)


def solution(mesh):
    assert mesh.devices.shape == (16, 32)
    fine = Mesh(mesh.devices.reshape(2, 4, 2, 2, 16), ALL)
    in_specs = (
        P(ALL, None),
        P(ALL),
        P(ALL, None),
        P(),
        P(REF, None),
    )
    out_specs = (P(REF, DOM), P(ALL))
    return jax.shard_map(
        per_device, mesh=fine, in_specs=in_specs, out_specs=out_specs, check_vma=False
    )
```

```python
import jax
import jax.numpy as jnp
from jax import lax
from jax.sharding import Mesh
from jax.sharding import PartitionSpec as P

SIDE = 64
REF = ("yh", "x", "c")
DOM = ("yl", "z")
ALL = REF + DOM
PLANE = ("yh", "x", "yl")


def shift_matrices(moves):
    line = jnp.arange(SIDE, dtype=jnp.int32)
    source = jnp.mod(line[None, :, None] - moves[:, None, None], SIDE)
    return (line[None, None, :] == source).astype(jnp.bfloat16)


def roll_set(images, offsets, sign):
    grid = images.reshape(images.shape[0], SIDE, SIDE)
    rows = shift_matrices(sign * offsets[:, 0])
    cols = shift_matrices(sign * offsets[:, 1])
    moved = jnp.einsum("sai,nij->snaj", rows, grid, preferred_element_type=jnp.float32).astype(jnp.bfloat16)
    moved = jnp.einsum("snaj,sbj->snab", moved, cols, preferred_element_type=jnp.float32).astype(jnp.bfloat16)
    return moved.reshape(offsets.shape[0], images.shape[0], SIDE * SIDE)


def partner(axis, size, bit):
    return [(i, i ^ bit) for i in range(size)]


def halve(t, axis, size, bit, dim):
    mine = (lax.axis_index(axis) // bit) % 2
    keep = lax.dynamic_index_in_dim(t, mine, dim, keepdims=False)
    send = lax.dynamic_index_in_dim(t, 1 - mine, dim, keepdims=False)
    return keep + lax.ppermute(send, axis, partner(axis, size, bit))


def halve_pair(t, first, second):
    mid = t.shape[2] // 2
    a = halve(halve(lax.slice_in_dim(t, 0, mid, axis=2), *first, 0), *second, 0)
    b = halve(halve(lax.slice_in_dim(t, mid, t.shape[2], axis=2), *second, 1), *first, 0)
    return jnp.concatenate([a, b], axis=0)


def class_half(weight, stacked, core):
    w = weight.reshape(*weight.shape[:2], 2, 2, 2, 2, 8)
    w = lax.dynamic_index_in_dim(w, core, 5, keepdims=False)
    half = jnp.einsum("psabci,spyzj->abciyzj", w, stacked.reshape(*stacked.shape[:2], 2, 16, 128),
                      preferred_element_type=jnp.float32)
    return half.transpose(0, 1, 2, 4, 5, 3, 6)


def reduce_blocks(weight, stacked):
    mine = lax.axis_index("c")
    sent = lax.ppermute(class_half(weight, stacked, 1 - mine), "c", partner("c", 2, 1))
    t = class_half(weight, stacked, mine) + sent
    t = t.reshape(-1, *t.shape[-3:])
    t = jnp.sum(lax.all_to_all(t, PLANE, 0, 0, tiled=True), axis=0)
    return jnp.sum(lax.all_to_all(t, "z", 0, 0, tiled=True), axis=0)


def gather_rows(rows):
    copies = jnp.broadcast_to(rows[None], (16, *rows.shape))
    return lax.all_to_all(copies, REF, 0, 0, tiled=True).reshape(-1, rows.shape[1])


def per_device(particles, inv_noise, candidates, offsets, references):
    tile_size = references.shape[0]
    all_classes = tile_size * 16
    stacked = roll_set(particles, offsets, -1)
    tile_rows = gather_rows(references)
    tile_float = tile_rows.astype(jnp.float32)
    norms = jnp.sum(tile_float * tile_float, axis=1)
    match_score = jnp.einsum(
        "spi,ji->psj", stacked, tile_rows, preferred_element_type=jnp.float32
    )
    update = match_score - 0.5 * norms[None, None, :]
    score = inv_noise[:, None, None] * update
    classes = jnp.arange(all_classes, dtype=jnp.int32)
    permitted_mask = jnp.any(candidates[:, :, None] == classes[None, None, :], axis=1)
    masked = jnp.where(permitted_mask[:, None, :], score, -1e30)
    peak_val = jnp.max(masked, axis=(1, 2))
    denom_sum = jnp.sum(jnp.exp(masked - peak_val[:, None, None]), axis=(1, 2))
    evidence = peak_val + jnp.log(denom_sum)
    weight = jnp.where(
        permitted_mask[:, None, :], jnp.exp(masked - evidence[:, None, None]), 0.0
    ).astype(jnp.bfloat16)
    shares = reduce_blocks(weight, stacked)
    row_power = jnp.sum(shares * shares, axis=1)
    row_power = row_power + lax.ppermute(row_power, "yl", partner("yl", 2, 1))
    row_power = jnp.broadcast_to(row_power[None], (16, row_power.shape[0]))
    row_power = jnp.sum(lax.all_to_all(row_power, "z", 0, 0, tiled=True), axis=0)
    refreshed = (shares / jnp.sqrt(row_power[:, None] / (SIDE * SIDE) + 1e-06)).astype(jnp.bfloat16)
    return (refreshed, evidence)


def solution(mesh):
    assert mesh.devices.shape == (16, 32)
    fine = Mesh(mesh.devices.reshape(2, 4, 2, 2, 16), ALL)
    in_specs = (
        P(ALL, None),
        P(ALL),
        P(ALL, None),
        P(),
        P(REF, None),
    )
    out_specs = (P(REF, DOM), P(ALL))
    return jax.shard_map(
        per_device, mesh=fine, in_specs=in_specs, out_specs=out_specs, check_vma=False
    )
```

```python
import jax
import jax.numpy as jnp
from jax import lax
from jax.sharding import Mesh
from jax.sharding import PartitionSpec as P

SIDE = 64
REF = ("yh", "x", "c")
DOM = ("yl", "z")
ALL = REF + DOM
PLANE = ("yh", "x", "yl")


def shift_matrices(moves):
    line = jnp.arange(SIDE, dtype=jnp.int32)
    source = jnp.mod(line[None, :, None] - moves[:, None, None], SIDE)
    return (line[None, None, :] == source).astype(jnp.bfloat16)


def roll_set(images, offsets, sign):
    grid = images.reshape(images.shape[0], SIDE, SIDE)
    rows = shift_matrices(sign * offsets[:, 0])
    cols = shift_matrices(sign * offsets[:, 1])
    moved = jnp.einsum("sai,nij->snaj", rows, grid, preferred_element_type=jnp.float32).astype(jnp.bfloat16)
    moved = jnp.einsum("snaj,sbj->snab", moved, cols, preferred_element_type=jnp.float32).astype(jnp.bfloat16)
    return moved.reshape(offsets.shape[0], images.shape[0], SIDE * SIDE)


def partner(axis, size, bit):
    return [(i, i ^ bit) for i in range(size)]


def halve(t, axis, size, bit, dim):
    mine = (lax.axis_index(axis) // bit) % 2
    keep = lax.dynamic_index_in_dim(t, mine, dim, keepdims=False)
    send = lax.dynamic_index_in_dim(t, 1 - mine, dim, keepdims=False)
    return keep + lax.ppermute(send, axis, partner(axis, size, bit))


def halve_pair(t, first, second):
    mid = t.shape[2] // 2
    a = halve(halve(lax.slice_in_dim(t, 0, mid, axis=2), *first, 0), *second, 0)
    b = halve(halve(lax.slice_in_dim(t, mid, t.shape[2], axis=2), *second, 1), *first, 0)
    return jnp.concatenate([a, b], axis=0)


def reduce_blocks(partial):
    t = partial.reshape(2, 2, 2, 2, 8, 2, 16, 128)
    t = t.transpose(3, 0, 1, 2, 5, 6, 4, 7)
    t = halve(t, "c", 2, 1, 0)
    t = t.reshape(-1, *t.shape[-3:])
    t = jnp.sum(lax.all_to_all(t, PLANE, 0, 0, tiled=True), axis=0)
    moved = lax.all_to_all(t.astype(jnp.bfloat16), "z", 0, 0, tiled=True)
    return jnp.sum(moved.astype(jnp.float32), axis=0)


def gather_rows(rows):
    copies = jnp.broadcast_to(rows[None], (16, *rows.shape))
    return lax.all_to_all(copies, REF, 0, 0, tiled=True).reshape(-1, rows.shape[1])


def per_device(particles, inv_noise, candidates, offsets, references):
    tile_size = references.shape[0]
    all_classes = tile_size * 16
    stacked = roll_set(particles, offsets, -1)
    tile_rows = gather_rows(references)
    tile_float = tile_rows.astype(jnp.float32)
    norms = jnp.sum(tile_float * tile_float, axis=1)
    match_score = jnp.einsum(
        "spi,ji->psj", stacked, tile_rows, preferred_element_type=jnp.float32
    )
    update = match_score - 0.5 * norms[None, None, :]
    score = inv_noise[:, None, None] * update
    classes = jnp.arange(all_classes, dtype=jnp.int32)
    permitted_mask = jnp.any(candidates[:, :, None] == classes[None, None, :], axis=1)
    masked = jnp.where(permitted_mask[:, None, :], score, -1e30)
    peak_val = jnp.max(masked, axis=(1, 2))
    denom_sum = jnp.sum(jnp.exp(masked - peak_val[:, None, None]), axis=(1, 2))
    evidence = peak_val + jnp.log(denom_sum)
    weight = jnp.where(
        permitted_mask[:, None, :], jnp.exp(masked - evidence[:, None, None]), 0.0
    ).astype(jnp.bfloat16)
    partial = jnp.einsum("psk,spq->kq", weight, stacked, preferred_element_type=jnp.float32)
    shares = reduce_blocks(partial)
    row_power = jnp.sum(shares * shares, axis=1)
    row_power = row_power + lax.ppermute(row_power, "yl", partner("yl", 2, 1))
    row_power = jnp.broadcast_to(row_power[None], (16, row_power.shape[0]))
    row_power = jnp.sum(lax.all_to_all(row_power, "z", 0, 0, tiled=True), axis=0)
    refreshed = (shares / jnp.sqrt(row_power[:, None] / (SIDE * SIDE) + 1e-06)).astype(jnp.bfloat16)
    return (refreshed, evidence)


def solution(mesh):
    assert mesh.devices.shape == (16, 32)
    fine = Mesh(mesh.devices.reshape(2, 4, 2, 2, 16), ALL)
    in_specs = (
        P(ALL, None),
        P(ALL),
        P(ALL, None),
        P(),
        P(REF, None),
    )
    out_specs = (P(REF, DOM), P(ALL))
    return jax.shard_map(
        per_device, mesh=fine, in_specs=in_specs, out_specs=out_specs, check_vma=False
    )
```

```python
import jax
import jax.numpy as jnp
from jax import lax
from jax.sharding import Mesh
from jax.sharding import PartitionSpec as P

SIDE = 64
REF = ("yh", "x", "c")
DOM = ("yl", "z")
ALL = REF + DOM
PLANE = ("yh", "x")


def shift_matrices(moves):
    line = jnp.arange(SIDE, dtype=jnp.int32)
    source = jnp.mod(line[None, :, None] - moves[:, None, None], SIDE)
    return (line[None, None, :] == source).astype(jnp.bfloat16)


def roll_set(images, offsets, sign):
    grid = images.reshape(images.shape[0], SIDE, SIDE)
    rows = shift_matrices(sign * offsets[:, 0])
    cols = shift_matrices(sign * offsets[:, 1])
    moved = jnp.einsum("sai,nij->snaj", rows, grid, preferred_element_type=jnp.float32).astype(jnp.bfloat16)
    moved = jnp.einsum("snaj,sbj->snab", moved, cols, preferred_element_type=jnp.float32).astype(jnp.bfloat16)
    return moved.reshape(offsets.shape[0], images.shape[0], SIDE * SIDE)


def partner(axis, size, bit):
    return [(i, i ^ bit) for i in range(size)]


def halve(t, axis, size, bit, dim):
    mine = (lax.axis_index(axis) // bit) % 2
    keep = lax.dynamic_index_in_dim(t, mine, dim, keepdims=False)
    send = lax.dynamic_index_in_dim(t, 1 - mine, dim, keepdims=False)
    return keep + lax.ppermute(send, axis, partner(axis, size, bit))


def halve_pair(t, first, second):
    mid = t.shape[2] // 2
    a = halve(halve(lax.slice_in_dim(t, 0, mid, axis=2), *first, 0), *second, 0)
    b = halve(halve(lax.slice_in_dim(t, mid, t.shape[2], axis=2), *second, 1), *first, 0)
    return jnp.concatenate([a, b], axis=0)


def reduce_blocks(partial):
    t = partial.reshape(2, 2, 2, 2, 8, 2, 16, 128)
    t = t.transpose(3, 0, 1, 2, 5, 6, 4, 7)
    t = halve(t, "c", 2, 1, 0)
    t = t.reshape(-1, 32, *t.shape[-2:])
    t = jnp.sum(lax.all_to_all(t, PLANE, 0, 0, tiled=True), axis=0)
    return jnp.sum(lax.all_to_all(t, DOM, 0, 0, tiled=True), axis=0)


def gather_rows(rows):
    copies = jnp.broadcast_to(rows[None], (16, *rows.shape))
    return lax.all_to_all(copies, REF, 0, 0, tiled=True).reshape(-1, rows.shape[1])


def per_device(particles, inv_noise, candidates, offsets, references):
    tile_size = references.shape[0]
    all_classes = tile_size * 16
    stacked = roll_set(particles, offsets, -1)
    tile_rows = gather_rows(references)
    tile_float = tile_rows.astype(jnp.float32)
    norms = jnp.sum(tile_float * tile_float, axis=1)
    match_score = jnp.einsum(
        "spi,ji->psj", stacked, tile_rows, preferred_element_type=jnp.float32
    )
    update = match_score - 0.5 * norms[None, None, :]
    score = inv_noise[:, None, None] * update
    classes = jnp.arange(all_classes, dtype=jnp.int32)
    permitted_mask = jnp.any(candidates[:, :, None] == classes[None, None, :], axis=1)
    masked = jnp.where(permitted_mask[:, None, :], score, -1e30)
    peak_val = jnp.max(masked, axis=(1, 2))
    denom_sum = jnp.sum(jnp.exp(masked - peak_val[:, None, None]), axis=(1, 2))
    evidence = peak_val + jnp.log(denom_sum)
    weight = jnp.where(
        permitted_mask[:, None, :], jnp.exp(masked - evidence[:, None, None]), 0.0
    ).astype(jnp.bfloat16)
    partial = jnp.einsum("psk,spq->kq", weight, stacked, preferred_element_type=jnp.float32)
    shares = reduce_blocks(partial)
    row_power = jnp.sum(shares * shares, axis=1)
    row_power = jnp.broadcast_to(row_power[None], (32, row_power.shape[0]))
    row_power = jnp.sum(lax.all_to_all(row_power, DOM, 0, 0, tiled=True), axis=0)
    refreshed = (shares / jnp.sqrt(row_power[:, None] / (SIDE * SIDE) + 1e-06)).astype(jnp.bfloat16)
    return (refreshed, evidence)


def solution(mesh):
    assert mesh.devices.shape == (16, 32)
    fine = Mesh(mesh.devices.reshape(2, 4, 2, 2, 16), ALL)
    in_specs = (
        P(ALL, None),
        P(ALL),
        P(ALL, None),
        P(),
        P(REF, None),
    )
    out_specs = (P(REF, DOM), P(ALL))
    return jax.shard_map(
        per_device, mesh=fine, in_specs=in_specs, out_specs=out_specs, check_vma=False
    )
```

```python
import jax
import jax.numpy as jnp
from jax import lax
from jax.sharding import Mesh
from jax.sharding import PartitionSpec as P

SIDE = 64
REF = ("yh", "x", "c")
DOM = ("yl", "z")
ALL = REF + DOM
PLANE = ("yh", "x", "c")


def shift_matrices(moves):
    line = jnp.arange(SIDE, dtype=jnp.int32)
    source = jnp.mod(line[None, :, None] - moves[:, None, None], SIDE)
    return (line[None, None, :] == source).astype(jnp.bfloat16)


def roll_set(images, offsets, sign):
    grid = images.reshape(images.shape[0], SIDE, SIDE)
    rows = shift_matrices(sign * offsets[:, 0])
    cols = shift_matrices(sign * offsets[:, 1])
    moved = jnp.einsum("sai,nij->snaj", rows, grid, preferred_element_type=jnp.float32).astype(jnp.bfloat16)
    moved = jnp.einsum("snaj,sbj->snab", moved, cols, preferred_element_type=jnp.float32).astype(jnp.bfloat16)
    return moved.reshape(offsets.shape[0], images.shape[0], SIDE * SIDE)


def partner(axis, size, bit):
    return [(i, i ^ bit) for i in range(size)]


def halve(t, axis, size, bit, dim):
    mine = (lax.axis_index(axis) // bit) % 2
    keep = lax.dynamic_index_in_dim(t, mine, dim, keepdims=False)
    send = lax.dynamic_index_in_dim(t, 1 - mine, dim, keepdims=False)
    return keep + lax.ppermute(send, axis, partner(axis, size, bit))


def halve_pair(t, first, second):
    mid = t.shape[2] // 2
    a = halve(halve(lax.slice_in_dim(t, 0, mid, axis=2), *first, 0), *second, 0)
    b = halve(halve(lax.slice_in_dim(t, mid, t.shape[2], axis=2), *second, 1), *first, 0)
    return jnp.concatenate([a, b], axis=0)


def reduce_blocks(partial):
    t = partial.reshape(2, 2, 2, 2, 8, 2, 16, 128)
    t = t.transpose(0, 1, 2, 3, 5, 6, 4, 7)
    t = t.reshape(-1, 32, *t.shape[-2:])
    t = jnp.sum(lax.all_to_all(t, PLANE, 0, 0, tiled=True), axis=0)
    return jnp.sum(lax.all_to_all(t, DOM, 0, 0, tiled=True), axis=0)


def gather_rows(rows):
    copies = jnp.broadcast_to(rows[None], (16, *rows.shape))
    return lax.all_to_all(copies, REF, 0, 0, tiled=True).reshape(-1, rows.shape[1])


def per_device(particles, inv_noise, candidates, offsets, references):
    tile_size = references.shape[0]
    all_classes = tile_size * 16
    stacked = roll_set(particles, offsets, -1)
    tile_rows = gather_rows(references)
    tile_float = tile_rows.astype(jnp.float32)
    norms = jnp.sum(tile_float * tile_float, axis=1)
    match_score = jnp.einsum(
        "spi,ji->psj", stacked, tile_rows, preferred_element_type=jnp.float32
    )
    update = match_score - 0.5 * norms[None, None, :]
    score = inv_noise[:, None, None] * update
    classes = jnp.arange(all_classes, dtype=jnp.int32)
    permitted_mask = jnp.any(candidates[:, :, None] == classes[None, None, :], axis=1)
    masked = jnp.where(permitted_mask[:, None, :], score, -1e30)
    peak_val = jnp.max(masked, axis=(1, 2))
    denom_sum = jnp.sum(jnp.exp(masked - peak_val[:, None, None]), axis=(1, 2))
    evidence = peak_val + jnp.log(denom_sum)
    weight = jnp.where(
        permitted_mask[:, None, :], jnp.exp(masked - evidence[:, None, None]), 0.0
    ).astype(jnp.bfloat16)
    partial = jnp.einsum("psk,spq->kq", weight, stacked, preferred_element_type=jnp.float32)
    shares = reduce_blocks(partial)
    row_power = jnp.sum(shares * shares, axis=1)
    row_power = jnp.broadcast_to(row_power[None], (32, row_power.shape[0]))
    row_power = jnp.sum(lax.all_to_all(row_power, DOM, 0, 0, tiled=True), axis=0)
    refreshed = (shares / jnp.sqrt(row_power[:, None] / (SIDE * SIDE) + 1e-06)).astype(jnp.bfloat16)
    return (refreshed, evidence)


def solution(mesh):
    assert mesh.devices.shape == (16, 32)
    fine = Mesh(mesh.devices.reshape(2, 4, 2, 2, 16), ALL)
    in_specs = (
        P(ALL, None),
        P(ALL),
        P(ALL, None),
        P(),
        P(REF, None),
    )
    out_specs = (P(REF, DOM), P(ALL))
    return jax.shard_map(
        per_device, mesh=fine, in_specs=in_specs, out_specs=out_specs, check_vma=False
    )
```
